128 devices in a mesh: expert: 32 (over y, z, core), ffn: 4 (over x).
Axes of the slice: x: 4, y: 4, z: 4, core: 2. Of those that a mesh axis runs over, the one named last changes fastest.
Arguments:
- tokens: bfloat16 [16384, 768], P('expert', 'ffn'), may hold values from -6 to 6
- cotangent: bfloat16 [16384, 768], P('expert', 'ffn'), may hold values from -6 to 6
- gates: float32 [16384, 2], P('expert'), may hold values from 0.2 to 1
- expert_ids: int32 [16384, 2], P('expert'), may hold values from 0 to 63, all different within a row; in each aligned block of 512 rows (0 to 511, 512 to 1023, ...) at most 32 rows name the same one
- up_weight: bfloat16 [64, 768, 3072], P('expert', None, 'ffn'), may hold values from -0.21875 to 0.21875
- down_weight: bfloat16 [64, 3072, 768], P('expert', 'ffn'), may hold values from -0.109375 to 0.109375
Outputs:
- layer_out: bfloat16 [16384, 768], P('expert', 'ffn')
- grad_tokens: bfloat16 [16384, 768], P('expert', 'ffn')
- grad_up: bfloat16 [64, 768, 3072], P('expert', None, 'ffn')
- grad_down: bfloat16 [64, 3072, 768], P('expert', 'ffn')
The draws below stay inside these ranges and needn't reach their ends.
Inputs may be any that keep to these rules, and one draw needn't show every extreme that they name: `expert_ids`: the two experts of a token differ. Among the tokens of one index of expert no expert is named more than 32 times, a bound that some block reaches.
All inputs are finite; a program needn't handle non-finite values.
Results may differ from the reference program's by a relative error of at most 0.0065.
Values may be sent and summed in bfloat16 or wider, within the bound.
No kernel may reach another device: no remote copies, remote signals or barrier semaphores. Data moves between devices by JAX's collectives and lax.ppermute only.
A program may use at most 192 MiB of HBM per device.

```python
import math
import jax
import jax.numpy as jnp
import numpy as np
from jax import lax

D = 768
FF = 3072
TOK_DEV = 512
EXPERTS = 64
TOKENS = 16384
CAP = 32
SLOTS = 1024
N_EXPERT = 32


def levels(rng, extent, pieces, least, top_value):
    def one(dim, blocks):
        heights = jax.random.uniform(jax.random.fold_in(jax.random.fold_in(rng, 6), dim), (blocks,), jnp.float32, least / len(pieces), top_value / len(pieces))
        return jnp.repeat(jnp.exp(heights), extent[dim] // blocks).reshape((-1,) + (1,) * (len(extent) - dim - 1))

    factor_of = one(*pieces[0])
    for cut in pieces[1:]:
        factor_of = factor_of * one(*cut)
    return factor_of


def shared_out(key, own, number, rows, number_of, top, reach, skew):
    sequence = jax.random.permutation(key, number_of)
    packed, usual = shares(number_of, rows * top, reach, skew, True), shares(number_of, rows * top, reach, skew, False)
    places = jnp.arange(number_of)

    def named(lengths, turn):
        used = int((lengths > 0).sum())
        fixed = max(1, used // 4)
        shifted = fixed + (places - fixed + turn * (used - fixed)) % max(1, number_of - fixed)
        return jnp.zeros((number_of,), jnp.int32).at[sequence[jnp.where(places < fixed, places, shifted)]].set(jnp.asarray(lengths, jnp.int32))

    lengths = jnp.where(number % 4 == 0, named(packed, number // 4), named(usual, number - number // 4 - 1))
    mixed = jax.random.permutation(jax.random.fold_in(own, 3), number_of)
    source_of, taker = mixed[0:number_of // 2 * 2:2], mixed[1:number_of // 2 * 2:2]
    slack = jnp.minimum(lengths[source_of] - 1, reach - lengths[taker]) // 2
    slack = jnp.where((source_of == sequence[0]) | (taker == sequence[0]) | (lengths[taker] == 0), 0, jnp.maximum(slack, 0))
    shifted = jax.random.randint(jax.random.fold_in(own, 4), (number_of // 2,), 0, 1 << 20) % (slack + 1)
    lengths = lengths.at[source_of].add(-shifted).at[taker].add(shifted)
    items = jnp.searchsorted(jnp.cumsum(lengths), jnp.arange(rows * top), side="right").astype(jnp.int32)
    table = items.reshape(top, rows).T
    table = table[jax.random.permutation(jax.random.fold_in(own, 1), rows)]
    turn = jax.random.randint(jax.random.fold_in(own, 2), (rows, 1), 0, top)
    return jnp.take_along_axis(table, (jnp.arange(top)[None, :] + turn) % top, axis=1)


def shares(number_of, total, bound, slope, full):
    portions = [(1 << 20) // math.isqrt(grade ** slope) + 1 for grade in range(1, number_of + 1)]
    largest = bound if full else min(bound, max(-(-total // number_of), total * portions[0] // sum(portions)))
    least = 1 if total - largest >= number_of - 1 else 0
    counts, surplus = [largest] + [least] * (number_of - 1), total - largest - least * (number_of - 1)
    while surplus > 0:
        movable = [i for i in range(1, number_of) if counts[i] < largest] or [i for i in range(1, number_of) if counts[i] < bound]
        whole, left = sum([portions[i] for i in movable]), surplus
        for i in movable:
            more = min(bound - counts[i], max(1, left * portions[i] // whole), surplus)
            counts[i] = counts[i] + more
            surplus = surplus - more
    return np.array(counts)


def normal_values(own_key, dims, width, reach, pieces=(), kind=jnp.bfloat16):
    values = width * jax.random.normal(own_key, dims, jnp.float32)
    if pieces:
        values = values * levels(own_key, dims, pieces, -0.22, 0.18)
    return jnp.clip(values, -reach, reach).astype(kind)


def setup_inputs(seed: int = 0) -> dict:
    keys = jax.random.split(jax.random.key(seed), 7)
    tokens = normal_values(keys[0], (TOKENS, D), 1.0, 6.0, ((0, 32), (1, 4)))
    cotangent = normal_values(keys[1], (TOKENS, D), 1.0, 6.0, ((0, 32), (1, 4)))
    gates = jnp.clip(jnp.exp(math.log(1.0) - 1.609438 * jax.random.uniform(keys[2], (TOKENS, 2), jnp.float32) ** levels(keys[2], (TOKENS, 2), ((0, 32),), -0.2, 0.2)), 0.2, 1.0)
    expert_ids_keys = jax.random.split(jax.random.fold_in(keys[3], 1), TOKENS // TOK_DEV)
    expert_ids_turns = jax.random.permutation(jax.random.fold_in(keys[3], 3), TOKENS // TOK_DEV)
    expert_ids = jax.vmap(lambda own, number: shared_out(jax.random.fold_in(keys[3], 2), own, number, TOK_DEV, EXPERTS, 2, CAP, 2))(expert_ids_keys, expert_ids_turns).reshape((TOKENS, 2))
    up_weight = normal_values(keys[4], (EXPERTS, D, FF), D ** -0.5, 0.21875, ((0, 32), (2, 4)))
    down_weight = normal_values(keys[5], (EXPERTS, FF, D), FF ** -0.5, 0.109375, ((0, 32), (1, 4)))
    return dict(tokens=tokens, cotangent=cotangent, gates=gates, expert_ids=expert_ids, up_weight=up_weight, down_weight=down_weight)


def reference(tokens, cotangent, gates, expert_ids, up_weight, down_weight):
    per_block = 2 * TOK_DEV
    flat_ids = expert_ids.reshape(N_EXPERT, per_block)
    labels = jnp.arange(EXPERTS, dtype=jnp.int32)
    onehot = (flat_ids[:, :, None] == labels[None, None, :]).astype(jnp.int32)
    before = jnp.cumsum(onehot, axis=1) - onehot
    position = jnp.sum(onehot * before, axis=2)
    slot_row = jnp.arange(N_EXPERT, dtype=jnp.int32)[:, None] * CAP + position
    table_key = (flat_ids * SLOTS + slot_row).reshape(-1)
    lookup = jnp.full((EXPERTS * SLOTS,), -1, jnp.int32).at[table_key].set(jnp.arange(2 * TOKENS, dtype=jnp.int32))
    scaled = (gates.reshape(-1)[:, None] * jnp.repeat(cotangent, 2, axis=0).astype(jnp.float32)).astype(tokens.dtype)
    zero_value = jnp.zeros((), tokens.dtype)

    def one_expert(expert):
        slot_index = lax.dynamic_slice_in_dim(lookup, expert * SLOTS, SLOTS)
        is_live = slot_index >= 0
        safe_index = jnp.where(is_live, slot_index, 0).astype(jnp.int32)
        rows_in = jnp.where(is_live[:, None], tokens[safe_index // 2], zero_value)
        grads_in = jnp.where(is_live[:, None], scaled[safe_index], zero_value)
        up_matrix = up_weight[expert]
        down_matrix = down_weight[expert]
        preact = jnp.dot(rows_in, up_matrix, preferred_element_type=jnp.float32)
        gating = jax.nn.sigmoid(preact)
        activated = (preact * gating).astype(tokens.dtype)
        expert_out = jnp.dot(activated, down_matrix, preferred_element_type=jnp.float32).astype(tokens.dtype)
        back_grad = jnp.dot(grads_in, down_matrix.T, preferred_element_type=jnp.float32)
        pre_grad = (back_grad * gating * (1.0 + preact * (1.0 - gating))).astype(tokens.dtype)
        grad_down = jnp.dot(activated.T, grads_in, preferred_element_type=jnp.float32).astype(tokens.dtype)
        grad_up = jnp.dot(rows_in.T, pre_grad, preferred_element_type=jnp.float32).astype(tokens.dtype)
        expert_in = jnp.dot(pre_grad, up_matrix.T, preferred_element_type=jnp.float32).astype(tokens.dtype)
        return grad_up, grad_down, expert_out, expert_in

    grad_up, grad_down, out_all, in_all = lax.map(one_expert, labels)
    all_ids = expert_ids.reshape(-1)
    all_rows = slot_row.reshape(-1)
    out_pick = out_all[all_ids, all_rows].astype(jnp.float32).reshape(TOKENS, 2, D)
    in_pick = in_all[all_ids, all_rows].astype(jnp.float32).reshape(TOKENS, 2, D)
    layer_out = jnp.sum(gates[:, :, None] * out_pick, axis=1).astype(tokens.dtype)
    grad_tokens = jnp.sum(in_pick, axis=1).astype(tokens.dtype)
    return layer_out, grad_tokens, grad_up, grad_down
```

```python
import jax
import jax.numpy as jnp
from jax import lax
from jax.experimental.layout import Layout, with_layout_constraint
from jax.sharding import PartitionSpec as P


def slot_targets(expert_ids, owners, local_experts, capacity):
    flat_ids = expert_ids.reshape(-1)
    count = flat_ids.shape[0]
    experts = owners * local_experts
    columns = lax.broadcasted_iota(jnp.int32, (count, experts), 1)
    onehot = (flat_ids[:, None] == columns).astype(jnp.bfloat16)
    earlier = (
        lax.broadcasted_iota(jnp.int32, (count, count), 0)
        > lax.broadcasted_iota(jnp.int32, (count, count), 1)
    ).astype(jnp.bfloat16)
    before = jnp.dot(earlier, onehot, preferred_element_type=jnp.float32)
    position = jnp.sum(onehot.astype(jnp.float32) * before, axis=1).astype(jnp.int32)
    return (flat_ids % local_experts) * (owners * capacity) + (flat_ids // local_experts) * capacity + position


def shards(tokens, cotangent, gates, expert_ids, up_weight, down_weight):
    owners = lax.axis_size("expert")
    local_experts = up_weight.shape[0]
    experts = owners * local_experts
    tok_rows = tokens.shape[0]
    capacity = 2 * tok_rows // owners
    rows = experts * capacity
    slots = owners * capacity
    target = slot_targets(expert_ids, owners, local_experts, capacity)
    row_ids = lax.broadcasted_iota(jnp.int32, (rows, 2 * tok_rows), 0)
    placer = (row_ids == target[None, :]).astype(jnp.bfloat16)
    tok_ids = lax.broadcasted_iota(jnp.int32, (rows, tok_rows), 0)
    pair = target.reshape(tok_rows, 2)
    token_placer = ((tok_ids == pair[None, :, 0]) | (tok_ids == pair[None, :, 1])).astype(
        jnp.bfloat16
    )
    weights = gates.reshape(-1)

    whole_tokens = lax.all_gather(tokens, "ffn", axis=1, tiled=True)
    whole_cot = lax.all_gather(cotangent, "ffn", axis=1, tiled=True)

    def dispatch(send):
        send = send.astype(jnp.bfloat16).reshape(local_experts, owners, capacity, send.shape[1])
        got = lax.all_to_all(send, "expert", split_axis=1, concat_axis=1, tiled=True)
        return got.reshape(local_experts, slots, got.shape[3])

    rows_in = dispatch(jnp.dot(token_placer, whole_tokens, preferred_element_type=jnp.float32))
    assigned = (weights[:, None] * jnp.repeat(whole_cot, 2, axis=0).astype(jnp.float32)).astype(
        jnp.bfloat16
    )
    grads_in = dispatch(jnp.dot(placer, assigned, preferred_element_type=jnp.float32))

    def send_home(parts):
        cols = jnp.stack(
            [
                lax.psum_scatter(
                    with_layout_constraint(part, Layout((0, 1))),
                    "ffn",
                    scatter_dimension=0,
                    tiled=True,
                )
                for part in parts
            ],
            axis=1,
        ).astype(jnp.bfloat16)
        cols = cols.reshape(cols.shape[0], local_experts, owners, capacity)
        back = lax.all_to_all(cols, "expert", split_axis=2, concat_axis=2, tiled=True)
        return back.reshape(back.shape[0], rows)

    preact = jnp.einsum("xsd,xdf->xsf", rows_in, up_weight, preferred_element_type=jnp.float32)
    gating = jax.nn.sigmoid(preact)
    activated = (preact * gating).astype(jnp.bfloat16)
    out_part = [
        jnp.einsum("fd,sf->ds", down_weight[x], activated[x], preferred_element_type=jnp.float32)
        for x in range(local_experts)
    ]
    out_home = send_home(out_part)
    back_grad = jnp.einsum(
        "xsd,xfd->xsf", grads_in, down_weight, preferred_element_type=jnp.float32
    )
    pre_grad = (back_grad * gating * (1.0 + preact * (1.0 - gating))).astype(jnp.bfloat16)
    grad_down = jnp.einsum(
        "xsf,xsd->xfd", activated, grads_in, preferred_element_type=jnp.float32
    ).astype(jnp.bfloat16)
    grad_up = jnp.einsum(
        "xsd,xsf->xdf", rows_in, pre_grad, preferred_element_type=jnp.float32
    ).astype(jnp.bfloat16)
    in_part = [
        jnp.einsum("df,sf->ds", up_weight[x], pre_grad[x], preferred_element_type=jnp.float32)
        for x in range(local_experts)
    ]
    in_home = send_home(in_part)

    def gather_back(returned):
        picked = lax.dot_general(
            placer, returned, (((0,), (1,)), ((), ())), preferred_element_type=jnp.float32
        )
        return picked.reshape(tok_rows, 2, returned.shape[0])

    layer_out = jnp.sum(gates[:, :, None] * gather_back(out_home), axis=1).astype(jnp.bfloat16)
    grad_tokens = jnp.sum(gather_back(in_home), axis=1).astype(jnp.bfloat16)
    return (layer_out, grad_tokens, grad_up, grad_down)


def solution(mesh):
    placed = (
        P("expert", "ffn"),
        P("expert", "ffn"),
        P("expert", None),
        P("expert", None),
        P("expert", None, "ffn"),
        P("expert", "ffn", None),
    )
    return jax.shard_map(
        shards,
        mesh=mesh,
        in_specs=placed,
        out_specs=(
            P("expert", "ffn"),
            P("expert", "ffn"),
            P("expert", None, "ffn"),
            P("expert", "ffn", None),
        ),
        check_vma=False,
    )
```

```python
import jax
import jax.numpy as jnp
from jax import lax
from jax.experimental.layout import Layout, with_layout_constraint
from jax.sharding import PartitionSpec as P


def slot_targets(expert_ids, owners, local_experts, capacity):
    flat_ids = expert_ids.reshape(-1)
    count = flat_ids.shape[0]
    experts = owners * local_experts
    columns = lax.broadcasted_iota(jnp.int32, (count, experts), 1)
    onehot = (flat_ids[:, None] == columns).astype(jnp.bfloat16)
    earlier = (
        lax.broadcasted_iota(jnp.int32, (count, count), 0)
        > lax.broadcasted_iota(jnp.int32, (count, count), 1)
    ).astype(jnp.bfloat16)
    before = jnp.dot(earlier, onehot, preferred_element_type=jnp.float32)
    position = jnp.sum(onehot.astype(jnp.float32) * before, axis=1).astype(jnp.int32)
    return (flat_ids % local_experts) * (owners * capacity) + (flat_ids // local_experts) * capacity + position


def shards(tokens, cotangent, gates, expert_ids, up_weight, down_weight):
    owners = lax.axis_size("expert")
    local_experts = up_weight.shape[0]
    experts = owners * local_experts
    tok_rows = tokens.shape[0]
    capacity = 2 * tok_rows // owners
    rows = experts * capacity
    slots = owners * capacity
    target = slot_targets(expert_ids, owners, local_experts, capacity)
    row_ids = lax.broadcasted_iota(jnp.int32, (rows, 2 * tok_rows), 0)
    placer = (row_ids == target[None, :]).astype(jnp.bfloat16)
    tok_ids = lax.broadcasted_iota(jnp.int32, (rows, tok_rows), 0)
    pair = target.reshape(tok_rows, 2)
    token_placer = ((tok_ids == pair[None, :, 0]) | (tok_ids == pair[None, :, 1])).astype(
        jnp.bfloat16
    )
    weights = gates.reshape(-1)

    whole_tokens = lax.all_gather(tokens, "ffn", axis=1, tiled=True)
    whole_cot = lax.all_gather(cotangent, "ffn", axis=1, tiled=True)

    def dispatch(send):
        send = send.astype(jnp.bfloat16).reshape(local_experts, owners, capacity, send.shape[1])
        got = lax.all_to_all(send, "expert", split_axis=1, concat_axis=1, tiled=True)
        return got.reshape(local_experts, slots, got.shape[3])

    rows_in = dispatch(jnp.dot(token_placer, whole_tokens, preferred_element_type=jnp.float32))
    assigned = (weights[:, None] * jnp.repeat(whole_cot, 2, axis=0).astype(jnp.float32)).astype(
        jnp.bfloat16
    )
    grads_in = dispatch(jnp.dot(placer, assigned, preferred_element_type=jnp.float32))

    def send_home(parts):
        cols = jnp.stack(
            [
                lax.psum_scatter(
                    with_layout_constraint(part, Layout((0, 1))).astype(jnp.bfloat16),
                    "ffn",
                    scatter_dimension=0,
                    tiled=True,
                )
                for part in parts
            ],
            axis=1,
        ).astype(jnp.bfloat16)
        cols = cols.reshape(cols.shape[0], local_experts, owners, capacity)
        back = lax.all_to_all(cols, "expert", split_axis=2, concat_axis=2, tiled=True)
        return back.reshape(back.shape[0], rows)

    preact = jnp.einsum("xsd,xdf->xsf", rows_in, up_weight, preferred_element_type=jnp.float32)
    gating = jax.nn.sigmoid(preact)
    activated = (preact * gating).astype(jnp.bfloat16)
    out_part = [
        jnp.einsum("fd,sf->ds", down_weight[x], activated[x], preferred_element_type=jnp.float32)
        for x in range(local_experts)
    ]
    out_home = send_home(out_part)
    back_grad = jnp.einsum(
        "xsd,xfd->xsf", grads_in, down_weight, preferred_element_type=jnp.float32
    )
    pre_grad = (back_grad * gating * (1.0 + preact * (1.0 - gating))).astype(jnp.bfloat16)
    grad_down = jnp.einsum(
        "xsf,xsd->xfd", activated, grads_in, preferred_element_type=jnp.float32
    ).astype(jnp.bfloat16)
    grad_up = jnp.einsum(
        "xsd,xsf->xdf", rows_in, pre_grad, preferred_element_type=jnp.float32
    ).astype(jnp.bfloat16)
    in_part = [
        jnp.einsum("df,sf->ds", up_weight[x], pre_grad[x], preferred_element_type=jnp.float32)
        for x in range(local_experts)
    ]
    in_home = send_home(in_part)

    def gather_back(returned):
        picked = lax.dot_general(
            placer, returned, (((0,), (1,)), ((), ())), preferred_element_type=jnp.float32
        )
        return picked.reshape(tok_rows, 2, returned.shape[0])

    layer_out = jnp.sum(gates[:, :, None] * gather_back(out_home), axis=1).astype(jnp.bfloat16)
    grad_tokens = jnp.sum(gather_back(in_home), axis=1).astype(jnp.bfloat16)
    return (layer_out, grad_tokens, grad_up, grad_down)


def solution(mesh):
    placed = (
        P("expert", "ffn"),
        P("expert", "ffn"),
        P("expert", None),
        P("expert", None),
        P("expert", None, "ffn"),
        P("expert", "ffn", None),
    )
    return jax.shard_map(
        shards,
        mesh=mesh,
        in_specs=placed,
        out_specs=(
            P("expert", "ffn"),
            P("expert", "ffn"),
            P("expert", None, "ffn"),
            P("expert", "ffn", None),
        ),
        check_vma=False,
    )
```

```python
import jax
import jax.numpy as jnp
from jax import lax
from jax.experimental.layout import Layout, with_layout_constraint
from jax.sharding import PartitionSpec as P


def slot_targets(expert_ids, owners, local_experts, capacity):
    flat_ids = expert_ids.reshape(-1)
    count = flat_ids.shape[0]
    experts = owners * local_experts
    columns = lax.broadcasted_iota(jnp.int32, (count, experts), 1)
    onehot = (flat_ids[:, None] == columns).astype(jnp.bfloat16)
    earlier = (
        lax.broadcasted_iota(jnp.int32, (count, count), 0)
        > lax.broadcasted_iota(jnp.int32, (count, count), 1)
    ).astype(jnp.bfloat16)
    before = jnp.dot(earlier, onehot, preferred_element_type=jnp.float32)
    position = jnp.sum(onehot.astype(jnp.float32) * before, axis=1).astype(jnp.int32)
    return (flat_ids % local_experts) * (owners * capacity) + (flat_ids // local_experts) * capacity + position


def shards(tokens, cotangent, gates, expert_ids, up_weight, down_weight):
    owners = lax.axis_size("expert")
    local_experts = up_weight.shape[0]
    experts = owners * local_experts
    tok_rows = tokens.shape[0]
    capacity = 2 * tok_rows // owners
    rows = experts * capacity
    slots = owners * capacity
    target = slot_targets(expert_ids, owners, local_experts, capacity)
    row_ids = lax.broadcasted_iota(jnp.int32, (rows, 2 * tok_rows), 0)
    placer = (row_ids == target[None, :]).astype(jnp.bfloat16)
    tok_ids = lax.broadcasted_iota(jnp.int32, (rows, tok_rows), 0)
    pair = target.reshape(tok_rows, 2)
    token_placer = ((tok_ids == pair[None, :, 0]) | (tok_ids == pair[None, :, 1])).astype(
        jnp.bfloat16
    )
    weights = gates.reshape(-1)

    width = tokens.shape[1]
    both = lax.all_gather(jnp.concatenate([tokens, cotangent], axis=1), "ffn", axis=1)
    whole_tokens = both[:, :, :width].reshape(tok_rows, -1)
    whole_cot = both[:, :, width:].reshape(tok_rows, -1)

    def dispatch(send):
        send = send.astype(jnp.bfloat16).reshape(local_experts, owners, capacity, send.shape[1])
        got = lax.all_to_all(send, "expert", split_axis=1, concat_axis=1, tiled=True)
        return got.reshape(local_experts, slots, got.shape[3])

    rows_in = dispatch(jnp.dot(token_placer, whole_tokens, preferred_element_type=jnp.float32))
    assigned = (gates[:, :, None] * whole_cot[:, None, :].astype(jnp.float32)).astype(jnp.bfloat16)
    assigned = assigned.reshape(2 * tok_rows, whole_cot.shape[1])
    grads_in = dispatch(jnp.dot(placer, assigned, preferred_element_type=jnp.float32))

    def send_home(parts):
        ffn = lax.axis_size("ffn")
        stacked = jnp.stack(
            [with_layout_constraint(part, Layout((0, 1))).astype(jnp.bfloat16) for part in parts],
            axis=1,
        )
        stacked = stacked.reshape(ffn, stacked.shape[0] // ffn, local_experts, slots)
        pieces = lax.all_to_all(stacked, "ffn", split_axis=0, concat_axis=0, tiled=True)
        cols = jnp.sum(pieces.astype(jnp.float32), axis=0).astype(jnp.bfloat16)
        cols = cols.reshape(cols.shape[0], local_experts, owners, capacity)
        back = lax.all_to_all(cols, "expert", split_axis=2, concat_axis=2, tiled=True)
        return back.reshape(back.shape[0], rows)

    preact = jnp.einsum("xsd,xdf->xsf", rows_in, up_weight, preferred_element_type=jnp.float32)
    gating = jax.nn.sigmoid(preact)
    activated = (preact * gating).astype(jnp.bfloat16)
    out_part = [
        jnp.einsum("fd,sf->ds", down_weight[x], activated[x], preferred_element_type=jnp.float32)
        for x in range(local_experts)
    ]
    out_home = send_home(out_part)
    back_grad = jnp.einsum(
        "xsd,xfd->xsf", grads_in, down_weight, preferred_element_type=jnp.float32
    )
    pre_grad = (back_grad * gating * (1.0 + preact * (1.0 - gating))).astype(jnp.bfloat16)
    grad_down = jnp.einsum(
        "xsf,xsd->xfd", activated, grads_in, preferred_element_type=jnp.float32
    ).astype(jnp.bfloat16)
    grad_up = jnp.einsum(
        "xsd,xsf->xdf", rows_in, pre_grad, preferred_element_type=jnp.float32
    ).astype(jnp.bfloat16)
    in_part = [
        jnp.einsum("df,sf->ds", up_weight[x], pre_grad[x], preferred_element_type=jnp.float32)
        for x in range(local_experts)
    ]
    in_home = send_home(in_part)

    def gather_back(returned):
        picked = lax.dot_general(
            placer, returned, (((0,), (1,)), ((), ())), preferred_element_type=jnp.float32
        )
        return picked.reshape(tok_rows, 2, returned.shape[0])

    layer_out = jnp.sum(gates[:, :, None] * gather_back(out_home), axis=1).astype(jnp.bfloat16)
    grad_tokens = jnp.sum(gather_back(in_home), axis=1).astype(jnp.bfloat16)
    return (layer_out, grad_tokens, grad_up, grad_down)


def solution(mesh):
    placed = (
        P("expert", "ffn"),
        P("expert", "ffn"),
        P("expert", None),
        P("expert", None),
        P("expert", None, "ffn"),
        P("expert", "ffn", None),
    )
    return jax.shard_map(
        shards,
        mesh=mesh,
        in_specs=placed,
        out_specs=(
            P("expert", "ffn"),
            P("expert", "ffn"),
            P("expert", None, "ffn"),
            P("expert", "ffn", None),
        ),
        check_vma=False,
    )
```

```python
import jax
import jax.numpy as jnp
from jax import lax
from jax.experimental.layout import Layout, with_layout_constraint
from jax.sharding import PartitionSpec as P


def slot_targets(expert_ids, owners, local_experts, capacity):
    flat_ids = expert_ids.reshape(-1)
    count = flat_ids.shape[0]
    experts = owners * local_experts
    columns = lax.broadcasted_iota(jnp.int32, (count, experts), 1)
    onehot = (flat_ids[:, None] == columns).astype(jnp.bfloat16)
    earlier = (
        lax.broadcasted_iota(jnp.int32, (count, count), 0)
        > lax.broadcasted_iota(jnp.int32, (count, count), 1)
    ).astype(jnp.bfloat16)
    before = jnp.dot(earlier, onehot, preferred_element_type=jnp.float32)
    position = jnp.sum(onehot.astype(jnp.float32) * before, axis=1).astype(jnp.int32)
    return (flat_ids % local_experts) * (owners * capacity) + (flat_ids // local_experts) * capacity + position


def shards(tokens, cotangent, gates, expert_ids, up_weight, down_weight):
    owners = lax.axis_size("expert")
    local_experts = up_weight.shape[0]
    experts = owners * local_experts
    tok_rows = tokens.shape[0]
    capacity = 2 * tok_rows // owners
    rows = experts * capacity
    slots = owners * capacity
    target = slot_targets(expert_ids, owners, local_experts, capacity)
    row_ids = lax.broadcasted_iota(jnp.int32, (rows, 2 * tok_rows), 0)
    placer = (row_ids == target[None, :]).astype(jnp.bfloat16)
    tok_ids = lax.broadcasted_iota(jnp.int32, (rows, tok_rows), 0)
    pair = target.reshape(tok_rows, 2)
    token_placer = ((tok_ids == pair[None, :, 0]) | (tok_ids == pair[None, :, 1])).astype(
        jnp.bfloat16
    )
    slot_gates = jnp.dot(
        placer.astype(jnp.float32),
        gates.reshape(-1),
        precision=lax.Precision.HIGHEST,
        preferred_element_type=jnp.float32,
    )

    whole_tokens = lax.all_gather(tokens, "ffn", axis=1, tiled=True)
    whole_cot = lax.all_gather(cotangent, "ffn", axis=1, tiled=True)

    def dispatch(send):
        send = send.reshape(local_experts, owners, capacity, *send.shape[1:])
        got = lax.all_to_all(send, "expert", split_axis=1, concat_axis=1, tiled=True)
        return got.reshape(local_experts, slots, *got.shape[3:])

    def place(whole):
        return jnp.dot(token_placer, whole, preferred_element_type=jnp.float32).astype(
            jnp.bfloat16
        )

    rows_in = dispatch(place(whole_tokens))
    cot_send = place(whole_cot)

    preact = jnp.einsum("xsd,xdf->xsf", rows_in, up_weight, preferred_element_type=jnp.float32)
    gating = jax.nn.sigmoid(preact)
    activated = (preact * gating).astype(jnp.bfloat16)
    out_part = [
        with_layout_constraint(
            jnp.einsum(
                "fd,sf->ds", down_weight[x], activated[x], preferred_element_type=jnp.float32
            ),
            Layout((0, 1)),
        ).astype(jnp.bfloat16)
        for x in range(local_experts)
    ]
    out_part, cot_send, slot_gates = lax.optimization_barrier((out_part, cot_send, slot_gates))

    cot_in = dispatch(cot_send)
    gate_in = dispatch(slot_gates)
    grads_in = (gate_in[:, :, None] * cot_in.astype(jnp.float32)).astype(jnp.bfloat16)

    def send_home(parts):
        cols = jnp.stack(
            [lax.psum_scatter(part, "ffn", scatter_dimension=0, tiled=True) for part in parts],
            axis=1,
        )
        cols = cols.reshape(cols.shape[0], local_experts, owners, capacity)
        back = lax.all_to_all(cols, "expert", split_axis=2, concat_axis=2, tiled=True)
        return back.reshape(back.shape[0], rows)

    out_home = send_home(out_part)
    back_grad = jnp.einsum(
        "xsd,xfd->xsf", grads_in, down_weight, preferred_element_type=jnp.float32
    )
    pre_grad = (back_grad * gating * (1.0 + preact * (1.0 - gating))).astype(jnp.bfloat16)
    grad_down = jnp.einsum(
        "xsf,xsd->xfd", activated, grads_in, preferred_element_type=jnp.float32
    ).astype(jnp.bfloat16)
    grad_up = jnp.einsum(
        "xsd,xsf->xdf", rows_in, pre_grad, preferred_element_type=jnp.float32
    ).astype(jnp.bfloat16)
    in_part = [
        with_layout_constraint(
            jnp.einsum(
                "df,sf->ds", up_weight[x], pre_grad[x], preferred_element_type=jnp.float32
            ),
            Layout((0, 1)),
        ).astype(jnp.bfloat16)
        for x in range(local_experts)
    ]
    in_home = send_home(in_part)

    def gather_back(returned):
        picked = lax.dot_general(
            placer, returned, (((0,), (1,)), ((), ())), preferred_element_type=jnp.float32
        )
        return picked.reshape(tok_rows, 2, returned.shape[0])

    layer_out = jnp.sum(gates[:, :, None] * gather_back(out_home), axis=1).astype(jnp.bfloat16)
    grad_tokens = jnp.sum(gather_back(in_home), axis=1).astype(jnp.bfloat16)
    return (layer_out, grad_tokens, grad_up, grad_down)


def solution(mesh):
    placed = (
        P("expert", "ffn"),
        P("expert", "ffn"),
        P("expert", None),
        P("expert", None),
        P("expert", None, "ffn"),
        P("expert", "ffn", None),
    )
    return jax.shard_map(
        shards,
        mesh=mesh,
        in_specs=placed,
        out_specs=(
            P("expert", "ffn"),
            P("expert", "ffn"),
            P("expert", None, "ffn"),
            P("expert", "ffn", None),
        ),
        check_vma=False,
    )
```

```python
import jax
import jax.numpy as jnp
from jax import lax
from jax.experimental.layout import Layout, with_layout_constraint
from jax.sharding import PartitionSpec as P


def slot_targets(expert_ids, owners, local_experts, capacity):
    flat_ids = expert_ids.reshape(-1)
    count = flat_ids.shape[0]
    experts = owners * local_experts
    columns = lax.broadcasted_iota(jnp.int32, (count, experts), 1)
    onehot = (flat_ids[:, None] == columns).astype(jnp.bfloat16)
    earlier = (
        lax.broadcasted_iota(jnp.int32, (count, count), 0)
        > lax.broadcasted_iota(jnp.int32, (count, count), 1)
    ).astype(jnp.bfloat16)
    before = jnp.dot(earlier, onehot, preferred_element_type=jnp.float32)
    position = jnp.sum(onehot.astype(jnp.float32) * before, axis=1).astype(jnp.int32)
    return (flat_ids % local_experts) * (owners * capacity) + (flat_ids // local_experts) * capacity + position


def shards(tokens, cotangent, gates, expert_ids, up_weight, down_weight):
    owners = lax.axis_size("expert")
    local_experts = up_weight.shape[0]
    experts = owners * local_experts
    tok_rows = tokens.shape[0]
    capacity = 2 * tok_rows // owners
    rows = experts * capacity
    slots = owners * capacity
    target = slot_targets(expert_ids, owners, local_experts, capacity)
    row_ids = lax.broadcasted_iota(jnp.int32, (rows, 2 * tok_rows), 0)
    placer = (row_ids == target[None, :]).astype(jnp.bfloat16)
    tok_ids = lax.broadcasted_iota(jnp.int32, (rows, tok_rows), 0)
    pair = target.reshape(tok_rows, 2)
    token_placer = ((tok_ids == pair[None, :, 0]) | (tok_ids == pair[None, :, 1])).astype(
        jnp.bfloat16
    )
    slot_gates = jnp.dot(
        placer.astype(jnp.float32),
        gates.reshape(-1),
        precision=lax.Precision.HIGHEST,
        preferred_element_type=jnp.float32,
    )

    whole_tokens = lax.all_gather(tokens, "ffn", axis=1, tiled=True)
    whole_cot = lax.all_gather(cotangent, "ffn", axis=1, tiled=True)

    def dispatch(send):
        send = send.reshape(local_experts, owners, capacity, *send.shape[1:])
        got = lax.all_to_all(send, "expert", split_axis=1, concat_axis=1, tiled=True)
        return got.reshape(local_experts, slots, *got.shape[3:])

    def place(whole):
        return jnp.dot(token_placer, whole, preferred_element_type=jnp.float32).astype(
            jnp.bfloat16
        )

    rows_in = dispatch(place(whole_tokens))
    scaled = slot_gates[:, None] * jnp.dot(
        token_placer, whole_cot, preferred_element_type=jnp.float32
    )
    rows_in, grads_send = lax.optimization_barrier((rows_in, scaled.astype(jnp.bfloat16)))
    grads_in = dispatch(grads_send)

    preact = jnp.einsum("xsd,xdf->xsf", rows_in, up_weight, preferred_element_type=jnp.float32)
    gating = jax.nn.sigmoid(preact)
    activated = (preact * gating).astype(jnp.bfloat16)
    out_part = [
        with_layout_constraint(
            jnp.einsum(
                "fd,sf->ds", down_weight[x], activated[x], preferred_element_type=jnp.float32
            ),
            Layout((0, 1)),
        ).astype(jnp.bfloat16)
        for x in range(local_experts)
    ]

    def send_home(parts):
        cols = jnp.stack(
            [lax.psum_scatter(part, "ffn", scatter_dimension=0, tiled=True) for part in parts],
            axis=1,
        )
        cols = cols.reshape(cols.shape[0], local_experts, owners, capacity)
        back = lax.all_to_all(cols, "expert", split_axis=2, concat_axis=2, tiled=True)
        return back.reshape(back.shape[0], rows)

    out_home = send_home(out_part)
    back_grad = jnp.einsum(
        "xsd,xfd->xsf", grads_in, down_weight, preferred_element_type=jnp.float32
    )
    pre_grad = (back_grad * gating * (1.0 + preact * (1.0 - gating))).astype(jnp.bfloat16)
    grad_down = jnp.einsum(
        "xsf,xsd->xfd", activated, grads_in, preferred_element_type=jnp.float32
    ).astype(jnp.bfloat16)
    grad_up = jnp.einsum(
        "xsd,xsf->xdf", rows_in, pre_grad, preferred_element_type=jnp.float32
    ).astype(jnp.bfloat16)
    in_part = [
        with_layout_constraint(
            jnp.einsum(
                "df,sf->ds", up_weight[x], pre_grad[x], preferred_element_type=jnp.float32
            ),
            Layout((0, 1)),
        ).astype(jnp.bfloat16)
        for x in range(local_experts)
    ]
    in_home = send_home(in_part)

    def gather_back(returned):
        picked = lax.dot_general(
            placer, returned, (((0,), (1,)), ((), ())), preferred_element_type=jnp.float32
        )
        return picked.reshape(tok_rows, 2, returned.shape[0])

    layer_out = jnp.sum(gates[:, :, None] * gather_back(out_home), axis=1).astype(jnp.bfloat16)
    grad_tokens = jnp.sum(gather_back(in_home), axis=1).astype(jnp.bfloat16)
    return (layer_out, grad_tokens, grad_up, grad_down)


def solution(mesh):
    placed = (
        P("expert", "ffn"),
        P("expert", "ffn"),
        P("expert", None),
        P("expert", None),
        P("expert", None, "ffn"),
        P("expert", "ffn", None),
    )
    return jax.shard_map(
        shards,
        mesh=mesh,
        in_specs=placed,
        out_specs=(
            P("expert", "ffn"),
            P("expert", "ffn"),
            P("expert", None, "ffn"),
            P("expert", "ffn", None),
        ),
        check_vma=False,
    )
```

```python
import jax
import jax.numpy as jnp
from jax import lax
from jax.experimental.layout import Layout, with_layout_constraint
from jax.sharding import PartitionSpec as P


def slot_targets(expert_ids, owners, local_experts, capacity):
    flat_ids = expert_ids.reshape(-1)
    count = flat_ids.shape[0]
    experts = owners * local_experts
    columns = lax.broadcasted_iota(jnp.int32, (count, experts), 1)
    onehot = (flat_ids[:, None] == columns).astype(jnp.bfloat16)
    earlier = (
        lax.broadcasted_iota(jnp.int32, (count, count), 0)
        > lax.broadcasted_iota(jnp.int32, (count, count), 1)
    ).astype(jnp.bfloat16)
    before = jnp.dot(earlier, onehot, preferred_element_type=jnp.float32)
    position = jnp.sum(onehot.astype(jnp.float32) * before, axis=1).astype(jnp.int32)
    return (flat_ids % local_experts) * (owners * capacity) + (flat_ids // local_experts) * capacity + position


def shards(tokens, cotangent, gates, expert_ids, up_weight, down_weight):
    owners = lax.axis_size("expert")
    local_experts = up_weight.shape[0]
    experts = owners * local_experts
    tok_rows = tokens.shape[0]
    capacity = 2 * tok_rows // owners
    rows = experts * capacity
    slots = owners * capacity
    target = slot_targets(expert_ids, owners, local_experts, capacity)
    row_ids = lax.broadcasted_iota(jnp.int32, (rows, 2 * tok_rows), 0)
    placer = (row_ids == target[None, :]).astype(jnp.bfloat16)
    tok_ids = lax.broadcasted_iota(jnp.int32, (rows, tok_rows), 0)
    pair = target.reshape(tok_rows, 2)
    token_placer = ((tok_ids == pair[None, :, 0]) | (tok_ids == pair[None, :, 1])).astype(
        jnp.bfloat16
    )
    slot_gates = jnp.dot(
        placer.astype(jnp.float32),
        gates.reshape(-1),
        precision=lax.Precision.HIGHEST,
        preferred_element_type=jnp.float32,
    )

    whole_tokens = lax.all_gather(tokens, "ffn", axis=1, tiled=True)
    whole_cot = lax.all_gather(cotangent, "ffn", axis=1, tiled=True)

    def dispatch(send):
        send = send.reshape(owners, capacity, *send.shape[1:])
        got = lax.all_to_all(send, "expert", split_axis=0, concat_axis=0, tiled=True)
        return got.reshape(slots, *got.shape[2:])

    def place(whole):
        return jnp.dot(token_placer, whole, preferred_element_type=jnp.float32)

    def send_home(part):
        cols = lax.psum_scatter(part, "ffn", scatter_dimension=0, tiled=True)
        cols = cols.reshape(cols.shape[0], owners, capacity)
        back = lax.all_to_all(cols, "expert", split_axis=1, concat_axis=1, tiled=True)
        return back.reshape(back.shape[0], slots)

    def gather_back(returned):
        picked = 0.0
        for x, got in enumerate(returned):
            picked = picked + lax.dot_general(
                placer[x * slots:(x + 1) * slots],
                got,
                (((0,), (1,)), ((), ())),
                preferred_element_type=jnp.float32,
            )
        return picked.reshape(tok_rows, 2, returned[0].shape[0])

    token_rows = place(whole_tokens).astype(jnp.bfloat16)
    grad_rows = (
        slot_gates[:, None] * place(whole_cot)
    ).astype(jnp.bfloat16)
    rows_in = []
    for x in range(local_experts):
        rows_in.append(dispatch(token_rows[x * slots:(x + 1) * slots]))
    *rows_in, grad_rows = lax.optimization_barrier((*rows_in, grad_rows))
    grads_in = []
    for x in range(local_experts):
        grads_in.append(dispatch(grad_rows[x * slots:(x + 1) * slots]))

    out_home, in_home, grad_up, grad_down = [], [], [], []
    for x in range(local_experts):
        preact = jnp.dot(rows_in[x], up_weight[x], preferred_element_type=jnp.float32)
        gating = jax.nn.sigmoid(preact)
        activated = (preact * gating).astype(jnp.bfloat16)
        out_part = with_layout_constraint(
            jnp.einsum("fd,sf->ds", down_weight[x], activated, preferred_element_type=jnp.float32),
            Layout((0, 1)),
        ).astype(jnp.bfloat16)
        out_home.append(send_home(out_part))
        back_grad = jnp.einsum(
            "sd,fd->sf", grads_in[x], down_weight[x], preferred_element_type=jnp.float32
        )
        pre_grad = (back_grad * gating * (1.0 + preact * (1.0 - gating))).astype(jnp.bfloat16)
        grad_down.append(
            jnp.einsum(
                "sf,sd->fd", activated, grads_in[x], preferred_element_type=jnp.float32
            ).astype(jnp.bfloat16)
        )
        grad_up.append(
            jnp.einsum(
                "sd,sf->df", rows_in[x], pre_grad, preferred_element_type=jnp.float32
            ).astype(jnp.bfloat16)
        )
        in_part = with_layout_constraint(
            jnp.einsum("df,sf->ds", up_weight[x], pre_grad, preferred_element_type=jnp.float32),
            Layout((0, 1)),
        ).astype(jnp.bfloat16)
        in_home.append(send_home(in_part))
    grad_up = jnp.stack(grad_up)
    grad_down = jnp.stack(grad_down)

    layer_out = jnp.sum(gates[:, :, None] * gather_back(out_home), axis=1).astype(jnp.bfloat16)
    grad_tokens = jnp.sum(gather_back(in_home), axis=1).astype(jnp.bfloat16)
    return (layer_out, grad_tokens, grad_up, grad_down)


def solution(mesh):
    placed = (
        P("expert", "ffn"),
        P("expert", "ffn"),
        P("expert", None),
        P("expert", None),
        P("expert", None, "ffn"),
        P("expert", "ffn", None),
    )
    return jax.shard_map(
        shards,
        mesh=mesh,
        in_specs=placed,
        out_specs=(
            P("expert", "ffn"),
            P("expert", "ffn"),
            P("expert", None, "ffn"),
            P("expert", "ffn", None),
        ),
        check_vma=False,
    )
```

```python
import jax
import jax.numpy as jnp
from jax import lax
from jax.experimental.layout import Layout, with_layout_constraint
from jax.sharding import PartitionSpec as P


def slot_targets(expert_ids, owners, local_experts, capacity):
    flat_ids = expert_ids.reshape(-1)
    count = flat_ids.shape[0]
    experts = owners * local_experts
    columns = lax.broadcasted_iota(jnp.int32, (count, experts), 1)
    onehot = (flat_ids[:, None] == columns).astype(jnp.bfloat16)
    earlier = (
        lax.broadcasted_iota(jnp.int32, (count, count), 0)
        > lax.broadcasted_iota(jnp.int32, (count, count), 1)
    ).astype(jnp.bfloat16)
    before = jnp.dot(earlier, onehot, preferred_element_type=jnp.float32)
    position = jnp.sum(onehot.astype(jnp.float32) * before, axis=1).astype(jnp.int32)
    return (flat_ids % local_experts) * (owners * capacity) + (flat_ids // local_experts) * capacity + position


def shards(tokens, cotangent, gates, expert_ids, up_weight, down_weight):
    owners = lax.axis_size("expert")
    local_experts = up_weight.shape[0]
    experts = owners * local_experts
    tok_rows = tokens.shape[0]
    capacity = 2 * tok_rows // owners
    rows = experts * capacity
    slots = owners * capacity
    target = slot_targets(expert_ids, owners, local_experts, capacity)
    row_ids = lax.broadcasted_iota(jnp.int32, (rows, 2 * tok_rows), 0)
    placer = (row_ids == target[None, :]).astype(jnp.bfloat16)
    tok_ids = lax.broadcasted_iota(jnp.int32, (rows, tok_rows), 0)
    pair = target.reshape(tok_rows, 2)
    token_placer = ((tok_ids == pair[None, :, 0]) | (tok_ids == pair[None, :, 1])).astype(
        jnp.bfloat16
    )
    slot_gates = jnp.dot(
        placer.astype(jnp.float32),
        gates.reshape(-1),
        precision=lax.Precision.HIGHEST,
        preferred_element_type=jnp.float32,
    )

    whole_tokens = lax.all_gather(tokens, "ffn", axis=1, tiled=True)
    whole_cot = lax.all_gather(cotangent, "ffn", axis=1, tiled=True)

    def dispatch(send):
        send = send.reshape(local_experts, owners, capacity, *send.shape[1:])
        got = lax.all_to_all(send, "expert", split_axis=1, concat_axis=1, tiled=True)
        return got.reshape(local_experts, slots, *got.shape[3:])

    def place(whole):
        return jnp.dot(token_placer, whole, preferred_element_type=jnp.float32).astype(
            jnp.bfloat16
        )

    rows_in = dispatch(place(whole_tokens))
    scaled = slot_gates[:, None] * jnp.dot(
        token_placer, whole_cot, preferred_element_type=jnp.float32
    )
    rows_in, grads_send = lax.optimization_barrier((rows_in, scaled.astype(jnp.bfloat16)))
    grads_in = dispatch(grads_send)

    preact = jnp.einsum("xsd,xdf->xsf", rows_in, up_weight, preferred_element_type=jnp.float32)
    gating = jax.nn.sigmoid(preact)
    activated = (preact * gating).astype(jnp.bfloat16)
    out_part = [
        with_layout_constraint(
            jnp.einsum(
                "fd,sf->ds", down_weight[x], activated[x], preferred_element_type=jnp.float32
            ),
            Layout((0, 1)),
        ).astype(jnp.bfloat16)
        for x in range(local_experts)
    ]

    def reduce_cols(part, on_sparse_core):
        if on_sparse_core:
            return lax.psum_scatter(part, "ffn", scatter_dimension=0, tiled=True)
        ffn = lax.axis_size("ffn")
        pieces = part.reshape(ffn, part.shape[0] // ffn, part.shape[1])
        pieces = lax.all_to_all(pieces, "ffn", split_axis=0, concat_axis=0, tiled=True)
        return jnp.sum(pieces.astype(jnp.float32), axis=0).astype(jnp.bfloat16)

    def send_home(parts, spread):
        cols = jnp.stack(
            [reduce_cols(part, not spread or x % 2 == 0) for x, part in enumerate(parts)],
            axis=1,
        )
        cols = cols.reshape(cols.shape[0], local_experts, owners, capacity)
        back = lax.all_to_all(cols, "expert", split_axis=2, concat_axis=2, tiled=True)
        return back.reshape(back.shape[0], rows)

    out_home = send_home(out_part, False)
    back_grad = jnp.einsum(
        "xsd,xfd->xsf", grads_in, down_weight, preferred_element_type=jnp.float32
    )
    pre_grad = (back_grad * gating * (1.0 + preact * (1.0 - gating))).astype(jnp.bfloat16)
    grad_down = jnp.einsum(
        "xsf,xsd->xfd", activated, grads_in, preferred_element_type=jnp.float32
    ).astype(jnp.bfloat16)
    grad_up = jnp.einsum(
        "xsd,xsf->xdf", rows_in, pre_grad, preferred_element_type=jnp.float32
    ).astype(jnp.bfloat16)
    in_part = [
        with_layout_constraint(
            jnp.einsum(
                "df,sf->ds", up_weight[x], pre_grad[x], preferred_element_type=jnp.float32
            ),
            Layout((0, 1)),
        ).astype(jnp.bfloat16)
        for x in range(local_experts)
    ]
    in_home = send_home(in_part, True)

    def gather_back(returned):
        picked = lax.dot_general(
            placer, returned, (((0,), (1,)), ((), ())), preferred_element_type=jnp.float32
        )
        return picked.reshape(tok_rows, 2, returned.shape[0])

    layer_out = jnp.sum(gates[:, :, None] * gather_back(out_home), axis=1).astype(jnp.bfloat16)
    grad_tokens = jnp.sum(gather_back(in_home), axis=1).astype(jnp.bfloat16)
    return (layer_out, grad_tokens, grad_up, grad_down)


def solution(mesh):
    placed = (
        P("expert", "ffn"),
        P("expert", "ffn"),
        P("expert", None),
        P("expert", None),
        P("expert", None, "ffn"),
        P("expert", "ffn", None),
    )
    return jax.shard_map(
        shards,
        mesh=mesh,
        in_specs=placed,
        out_specs=(
            P("expert", "ffn"),
            P("expert", "ffn"),
            P("expert", None, "ffn"),
            P("expert", "ffn", None),
        ),
        check_vma=False,
    )
```

```python
import jax
import jax.numpy as jnp
from jax import lax
from jax.experimental.layout import Layout, with_layout_constraint
from jax.sharding import PartitionSpec as P


def slot_targets(expert_ids, owners, local_experts, capacity):
    flat_ids = expert_ids.reshape(-1)
    count = flat_ids.shape[0]
    experts = owners * local_experts
    columns = lax.broadcasted_iota(jnp.int32, (count, experts), 1)
    onehot = (flat_ids[:, None] == columns).astype(jnp.bfloat16)
    earlier = (
        lax.broadcasted_iota(jnp.int32, (count, count), 0)
        > lax.broadcasted_iota(jnp.int32, (count, count), 1)
    ).astype(jnp.bfloat16)
    before = jnp.dot(earlier, onehot, preferred_element_type=jnp.float32)
    position = jnp.sum(onehot.astype(jnp.float32) * before, axis=1).astype(jnp.int32)
    return (flat_ids % local_experts) * (owners * capacity) + (flat_ids // local_experts) * capacity + position


def shards(tokens, cotangent, gates, expert_ids, up_weight, down_weight):
    owners = lax.axis_size("expert")
    local_experts = up_weight.shape[0]
    experts = owners * local_experts
    tok_rows = tokens.shape[0]
    capacity = 2 * tok_rows // owners
    rows = experts * capacity
    slots = owners * capacity
    target = slot_targets(expert_ids, owners, local_experts, capacity)
    row_ids = lax.broadcasted_iota(jnp.int32, (rows, 2 * tok_rows), 0)
    placer = (row_ids == target[None, :]).astype(jnp.bfloat16)
    tok_ids = lax.broadcasted_iota(jnp.int32, (rows, tok_rows), 0)
    pair = target.reshape(tok_rows, 2)
    token_placer = ((tok_ids == pair[None, :, 0]) | (tok_ids == pair[None, :, 1])).astype(
        jnp.bfloat16
    )
    slot_gates = jnp.dot(
        placer.astype(jnp.float32),
        gates.reshape(-1),
        precision=lax.Precision.HIGHEST,
        preferred_element_type=jnp.float32,
    )

    whole_tokens = lax.all_gather(tokens, "ffn", axis=1, tiled=True)
    whole_cot = lax.all_gather(cotangent, "ffn", axis=1, tiled=True)

    def dispatch(send):
        send = send.reshape(local_experts, owners, capacity, *send.shape[1:])
        got = lax.all_to_all(send, "expert", split_axis=1, concat_axis=1, tiled=True)
        return got.reshape(local_experts, slots, *got.shape[3:])

    def place(whole):
        return jnp.dot(token_placer, whole, preferred_element_type=jnp.float32).astype(
            jnp.bfloat16
        )

    rows_in = dispatch(place(whole_tokens))
    scaled = slot_gates[:, None] * jnp.dot(
        token_placer, whole_cot, preferred_element_type=jnp.float32
    )
    rows_in, grads_send = lax.optimization_barrier((rows_in, scaled.astype(jnp.bfloat16)))
    grads_in = dispatch(grads_send)

    preact = jnp.einsum("xsd,xdf->xsf", rows_in, up_weight, preferred_element_type=jnp.float32)
    gating = jax.nn.sigmoid(preact)
    activated = (preact * gating).astype(jnp.bfloat16)
    out_part = [
        with_layout_constraint(
            jnp.einsum(
                "fd,sf->ds", down_weight[x], activated[x], preferred_element_type=jnp.float32
            ),
            Layout((0, 1)),
        ).astype(jnp.bfloat16)
        for x in range(local_experts)
    ]

    def ring_reduce(parts):
        ffn = lax.axis_size("ffn")
        me = lax.axis_index("ffn")
        sums = []
        for x, part in enumerate(parts):
            way = 1 if x % 2 == 0 else -1
            chunks = part.reshape(ffn, part.shape[0] // ffn, part.shape[1])
            order = (me - way * jnp.arange(1, ffn + 1, dtype=jnp.int32)) % ffn
            chunks = jnp.take(chunks, order, axis=0)
            perm = [(i, (i + way) % ffn) for i in range(ffn)]
            acc = chunks[0].astype(jnp.float32)
            for step in range(1, ffn):
                acc = lax.ppermute(acc.astype(jnp.bfloat16), "ffn", perm).astype(jnp.float32)
                acc = acc + chunks[step].astype(jnp.float32)
            sums.append(acc.astype(jnp.bfloat16))
        return sums

    def send_home(parts, ring):
        if ring:
            cols = jnp.stack(ring_reduce(parts), axis=1)
        else:
            cols = jnp.stack(
                [lax.psum_scatter(p, "ffn", scatter_dimension=0, tiled=True) for p in parts],
                axis=1,
            )
        cols = cols.reshape(cols.shape[0], local_experts, owners, capacity)
        back = lax.all_to_all(cols, "expert", split_axis=2, concat_axis=2, tiled=True)
        return back.reshape(back.shape[0], rows)

    out_home = send_home(out_part, False)
    back_grad = jnp.einsum(
        "xsd,xfd->xsf", grads_in, down_weight, preferred_element_type=jnp.float32
    )
    pre_grad = (back_grad * gating * (1.0 + preact * (1.0 - gating))).astype(jnp.bfloat16)
    grad_down = jnp.einsum(
        "xsf,xsd->xfd", activated, grads_in, preferred_element_type=jnp.float32
    ).astype(jnp.bfloat16)
    grad_up = jnp.einsum(
        "xsd,xsf->xdf", rows_in, pre_grad, preferred_element_type=jnp.float32
    ).astype(jnp.bfloat16)
    in_part = [
        with_layout_constraint(
            jnp.einsum(
                "df,sf->ds", up_weight[x], pre_grad[x], preferred_element_type=jnp.float32
            ),
            Layout((0, 1)),
        ).astype(jnp.bfloat16)
        for x in range(local_experts)
    ]
    in_home = send_home(in_part, True)

    def gather_back(returned):
        picked = lax.dot_general(
            placer, returned, (((0,), (1,)), ((), ())), preferred_element_type=jnp.float32
        )
        return picked.reshape(tok_rows, 2, returned.shape[0])

    layer_out = jnp.sum(gates[:, :, None] * gather_back(out_home), axis=1).astype(jnp.bfloat16)
    grad_tokens = jnp.sum(gather_back(in_home), axis=1).astype(jnp.bfloat16)
    return (layer_out, grad_tokens, grad_up, grad_down)


def solution(mesh):
    placed = (
        P("expert", "ffn"),
        P("expert", "ffn"),
        P("expert", None),
        P("expert", None),
        P("expert", None, "ffn"),
        P("expert", "ffn", None),
    )
    return jax.shard_map(
        shards,
        mesh=mesh,
        in_specs=placed,
        out_specs=(
            P("expert", "ffn"),
            P("expert", "ffn"),
            P("expert", None, "ffn"),
            P("expert", "ffn", None),
        ),
        check_vma=False,
    )
```

```python
import jax
import jax.numpy as jnp
from jax import lax
from jax.experimental.layout import Layout, with_layout_constraint
from jax.sharding import PartitionSpec as P


def slot_targets(expert_ids, owners, local_experts, capacity):
    flat_ids = expert_ids.reshape(-1)
    count = flat_ids.shape[0]
    experts = owners * local_experts
    columns = lax.broadcasted_iota(jnp.int32, (count, experts), 1)
    onehot = (flat_ids[:, None] == columns).astype(jnp.bfloat16)
    earlier = (
        lax.broadcasted_iota(jnp.int32, (count, count), 0)
        > lax.broadcasted_iota(jnp.int32, (count, count), 1)
    ).astype(jnp.bfloat16)
    before = jnp.dot(earlier, onehot, preferred_element_type=jnp.float32)
    position = jnp.sum(onehot.astype(jnp.float32) * before, axis=1).astype(jnp.int32)
    return (flat_ids % local_experts) * (owners * capacity) + (flat_ids // local_experts) * capacity + position


def shards(tokens, cotangent, gates, expert_ids, up_weight, down_weight):
    owners = lax.axis_size("expert")
    local_experts = up_weight.shape[0]
    experts = owners * local_experts
    tok_rows = tokens.shape[0]
    capacity = 2 * tok_rows // owners
    rows = experts * capacity
    slots = owners * capacity
    target = slot_targets(expert_ids, owners, local_experts, capacity)
    row_ids = lax.broadcasted_iota(jnp.int32, (rows, 2 * tok_rows), 0)
    placer = (row_ids == target[None, :]).astype(jnp.bfloat16)
    tok_ids = lax.broadcasted_iota(jnp.int32, (rows, tok_rows), 0)
    pair = target.reshape(tok_rows, 2)
    token_placer = ((tok_ids == pair[None, :, 0]) | (tok_ids == pair[None, :, 1])).astype(
        jnp.bfloat16
    )
    slot_gates = jnp.dot(
        placer.astype(jnp.float32),
        gates.reshape(-1),
        precision=lax.Precision.HIGHEST,
        preferred_element_type=jnp.float32,
    )

    whole_tokens = lax.all_gather(tokens, "ffn", axis=1, tiled=True)
    whole_cot = lax.all_gather(cotangent, "ffn", axis=1, tiled=True)

    def dispatch(send):
        send = send.reshape(local_experts, owners, capacity, *send.shape[1:])
        got = lax.all_to_all(send, "expert", split_axis=1, concat_axis=1, tiled=True)
        return got.reshape(local_experts, slots, *got.shape[3:])

    def place(whole):
        return jnp.dot(token_placer, whole, preferred_element_type=jnp.float32).astype(
            jnp.bfloat16
        )

    rows_in = dispatch(place(whole_tokens))
    scaled = slot_gates[:, None] * jnp.dot(
        token_placer, whole_cot, preferred_element_type=jnp.float32
    )
    rows_in, grads_send = lax.optimization_barrier((rows_in, scaled.astype(jnp.bfloat16)))
    grads_in = dispatch(grads_send)

    preact = jnp.einsum("xsd,xdf->xsf", rows_in, up_weight, preferred_element_type=jnp.float32)
    gating = jax.nn.sigmoid(preact)
    activated = (preact * gating).astype(jnp.bfloat16)
    out_part = [
        with_layout_constraint(
            jnp.einsum(
                "fd,sf->ds", down_weight[x], activated[x], preferred_element_type=jnp.float32
            ),
            Layout((0, 1)),
        ).astype(jnp.bfloat16)
        for x in range(local_experts)
    ]

    def ring_reduce(parts):
        ffn = lax.axis_size("ffn")
        me = lax.axis_index("ffn")
        sums = []
        for x, part in enumerate(parts):
            way = 1 if x % 2 == 0 else -1
            chunks = part.reshape(ffn, part.shape[0] // ffn, part.shape[1])
            order = (me - way * jnp.arange(1, ffn + 1, dtype=jnp.int32)) % ffn
            chunks = jnp.take(chunks, order, axis=0)
            perm = [(i, (i + way) % ffn) for i in range(ffn)]
            acc = chunks[0].astype(jnp.float32)
            for step in range(1, ffn):
                acc = lax.ppermute(acc.astype(jnp.bfloat16), "ffn", perm).astype(jnp.float32)
                acc = acc + chunks[step].astype(jnp.float32)
            sums.append(acc.astype(jnp.bfloat16))
        return sums

    def send_home(parts, ring):
        if ring:
            cols = jnp.stack(ring_reduce(parts), axis=1)
        else:
            cols = jnp.stack(
                [lax.psum_scatter(p, "ffn", scatter_dimension=0, tiled=True) for p in parts],
                axis=1,
            )
        cols = cols.reshape(cols.shape[0], local_experts, owners, capacity)
        back = lax.all_to_all(cols, "expert", split_axis=2, concat_axis=2, tiled=True)
        return back.reshape(back.shape[0], rows)

    out_home = send_home(out_part, False)
    back_grad = jnp.einsum(
        "xsd,xfd->xsf", grads_in, down_weight, preferred_element_type=jnp.float32
    )
    pre_grad = (back_grad * gating * (1.0 + preact * (1.0 - gating))).astype(jnp.bfloat16)
    grad_down = jnp.einsum(
        "xsf,xsd->xfd", activated, grads_in, preferred_element_type=jnp.float32
    ).astype(jnp.bfloat16)
    grad_up = jnp.einsum(
        "xsd,xsf->xdf", rows_in, pre_grad, preferred_element_type=jnp.float32
    ).astype(jnp.bfloat16)
    in_part = [
        with_layout_constraint(
            jnp.einsum(
                "df,sf->ds", up_weight[x], pre_grad[x], preferred_element_type=jnp.float32
            ),
            Layout((0, 1)),
        ).astype(jnp.bfloat16)
        for x in range(local_experts)
    ]
    in_home = send_home(in_part, True)

    def gather_back(returned):
        picked = jnp.take(returned.T, target, axis=0).astype(jnp.float32)
        return picked.reshape(tok_rows, 2, returned.shape[0])

    layer_out = jnp.sum(gates[:, :, None] * gather_back(out_home), axis=1).astype(jnp.bfloat16)
    grad_tokens = jnp.sum(gather_back(in_home), axis=1).astype(jnp.bfloat16)
    return (layer_out, grad_tokens, grad_up, grad_down)


def solution(mesh):
    placed = (
        P("expert", "ffn"),
        P("expert", "ffn"),
        P("expert", None),
        P("expert", None),
        P("expert", None, "ffn"),
        P("expert", "ffn", None),
    )
    return jax.shard_map(
        shards,
        mesh=mesh,
        in_specs=placed,
        out_specs=(
            P("expert", "ffn"),
            P("expert", "ffn"),
            P("expert", None, "ffn"),
            P("expert", "ffn", None),
        ),
        check_vma=False,
    )
```

```python
import jax
import jax.numpy as jnp
from jax import lax
from jax.experimental.layout import Layout, with_layout_constraint
from jax.sharding import PartitionSpec as P


def slot_targets(expert_ids, owners, local_experts, capacity):
    flat_ids = expert_ids.reshape(-1)
    count = flat_ids.shape[0]
    experts = owners * local_experts
    columns = lax.broadcasted_iota(jnp.int32, (count, experts), 1)
    onehot = (flat_ids[:, None] == columns).astype(jnp.bfloat16)
    earlier = (
        lax.broadcasted_iota(jnp.int32, (count, count), 0)
        > lax.broadcasted_iota(jnp.int32, (count, count), 1)
    ).astype(jnp.bfloat16)
    before = jnp.dot(earlier, onehot, preferred_element_type=jnp.float32)
    position = jnp.sum(onehot.astype(jnp.float32) * before, axis=1).astype(jnp.int32)
    return (flat_ids % local_experts) * (owners * capacity) + (flat_ids // local_experts) * capacity + position


def shards(tokens, cotangent, gates, expert_ids, up_weight, down_weight):
    owners = lax.axis_size("expert")
    local_experts = up_weight.shape[0]
    experts = owners * local_experts
    tok_rows = tokens.shape[0]
    capacity = 2 * tok_rows // owners
    rows = experts * capacity
    slots = owners * capacity
    target = slot_targets(expert_ids, owners, local_experts, capacity)
    row_ids = lax.broadcasted_iota(jnp.int32, (rows, 2 * tok_rows), 0)
    placer = (row_ids == target[None, :]).astype(jnp.bfloat16)
    tok_ids = lax.broadcasted_iota(jnp.int32, (rows, tok_rows), 0)
    pair = target.reshape(tok_rows, 2)
    token_placer = ((tok_ids == pair[None, :, 0]) | (tok_ids == pair[None, :, 1])).astype(
        jnp.bfloat16
    )
    slot_gates = jnp.dot(
        placer.astype(jnp.float32),
        gates.reshape(-1),
        precision=lax.Precision.HIGHEST,
        preferred_element_type=jnp.float32,
    )

    whole_tokens = lax.all_gather(tokens, "ffn", axis=1, tiled=True)
    whole_cot = lax.all_gather(cotangent, "ffn", axis=1, tiled=True)

    def dispatch(send):
        send = send.reshape(local_experts, owners, capacity, *send.shape[1:])
        got = lax.all_to_all(send, "expert", split_axis=1, concat_axis=1, tiled=True)
        return got.reshape(local_experts, slots, *got.shape[3:])

    def place(whole):
        return jnp.dot(token_placer, whole, preferred_element_type=jnp.float32).astype(
            jnp.bfloat16
        )

    rows_in = dispatch(place(whole_tokens))
    scaled = slot_gates[:, None] * jnp.dot(
        token_placer, whole_cot, preferred_element_type=jnp.float32
    )
    rows_in, grads_send = lax.optimization_barrier((rows_in, scaled.astype(jnp.bfloat16)))
    grads_in = dispatch(grads_send)

    preact = jnp.einsum("xsd,xdf->xsf", rows_in, up_weight, preferred_element_type=jnp.float32)
    gating = jax.nn.sigmoid(preact)
    activated = (preact * gating).astype(jnp.bfloat16)
    out_part = [
        with_layout_constraint(
            jnp.einsum(
                "fd,sf->ds", down_weight[x], activated[x], preferred_element_type=jnp.float32
            ),
            Layout((0, 1)),
        ).astype(jnp.bfloat16)
        for x in range(local_experts)
    ]

    def ring_reduce(parts):
        ffn = lax.axis_size("ffn")
        me = lax.axis_index("ffn")
        sums = []
        for x, part in enumerate(parts):
            way = 1 if x % 2 == 0 else -1
            chunks = part.reshape(ffn, part.shape[0] // ffn, part.shape[1])
            order = (me - way * jnp.arange(1, ffn + 1, dtype=jnp.int32)) % ffn
            chunks = jnp.take(chunks, order, axis=0)
            perm = [(i, (i + way) % ffn) for i in range(ffn)]
            acc = chunks[0].astype(jnp.float32)
            for step in range(1, ffn):
                acc = lax.ppermute(acc.astype(jnp.bfloat16), "ffn", perm).astype(jnp.float32)
                acc = acc + chunks[step].astype(jnp.float32)
            sums.append(acc.astype(jnp.bfloat16))
        return sums

    def reduce_home(parts, ring):
        if ring:
            return jnp.stack(ring_reduce(parts), axis=1)
        return jnp.stack(
            [lax.psum_scatter(p, "ffn", scatter_dimension=0, tiled=True) for p in parts],
            axis=1,
        )

    def send_home(both):
        both = both.reshape(*both.shape[:3], owners, capacity)
        back = lax.all_to_all(both, "expert", split_axis=3, concat_axis=3, tiled=True)
        return back.reshape(*back.shape[:2], rows)

    out_cols = reduce_home(out_part, False)
    back_grad = jnp.einsum(
        "xsd,xfd->xsf", grads_in, down_weight, preferred_element_type=jnp.float32
    )
    pre_grad = (back_grad * gating * (1.0 + preact * (1.0 - gating))).astype(jnp.bfloat16)
    grad_down = jnp.einsum(
        "xsf,xsd->xfd", activated, grads_in, preferred_element_type=jnp.float32
    ).astype(jnp.bfloat16)
    grad_up = jnp.einsum(
        "xsd,xsf->xdf", rows_in, pre_grad, preferred_element_type=jnp.float32
    ).astype(jnp.bfloat16)
    in_part = [
        with_layout_constraint(
            jnp.einsum(
                "df,sf->ds", up_weight[x], pre_grad[x], preferred_element_type=jnp.float32
            ),
            Layout((0, 1)),
        ).astype(jnp.bfloat16)
        for x in range(local_experts)
    ]
    in_cols = reduce_home(in_part, True)
    out_home, in_home = send_home(jnp.stack([out_cols, in_cols]))

    def gather_back(returned):
        picked = jnp.take(returned.T, target, axis=0).astype(jnp.float32)
        return picked.reshape(tok_rows, 2, returned.shape[0])

    layer_out = jnp.sum(gates[:, :, None] * gather_back(out_home), axis=1).astype(jnp.bfloat16)
    grad_tokens = jnp.sum(gather_back(in_home), axis=1).astype(jnp.bfloat16)
    return (layer_out, grad_tokens, grad_up, grad_down)


def solution(mesh):
    placed = (
        P("expert", "ffn"),
        P("expert", "ffn"),
        P("expert", None),
        P("expert", None),
        P("expert", None, "ffn"),
        P("expert", "ffn", None),
    )
    return jax.shard_map(
        shards,
        mesh=mesh,
        in_specs=placed,
        out_specs=(
            P("expert", "ffn"),
            P("expert", "ffn"),
            P("expert", None, "ffn"),
            P("expert", "ffn", None),
        ),
        check_vma=False,
    )
```

```python
import jax
import jax.numpy as jnp
from jax import lax
from jax.experimental.layout import Layout, with_layout_constraint
from jax.sharding import PartitionSpec as P


def slot_targets(expert_ids, owners, local_experts, capacity):
    flat_ids = expert_ids.reshape(-1)
    count = flat_ids.shape[0]
    experts = owners * local_experts
    columns = lax.broadcasted_iota(jnp.int32, (count, experts), 1)
    onehot = (flat_ids[:, None] == columns).astype(jnp.bfloat16)
    earlier = (
        lax.broadcasted_iota(jnp.int32, (count, count), 0)
        > lax.broadcasted_iota(jnp.int32, (count, count), 1)
    ).astype(jnp.bfloat16)
    before = jnp.dot(earlier, onehot, preferred_element_type=jnp.float32)
    position = jnp.sum(onehot.astype(jnp.float32) * before, axis=1).astype(jnp.int32)
    return (flat_ids % local_experts) * (owners * capacity) + (flat_ids // local_experts) * capacity + position


def shards(tokens, cotangent, gates, expert_ids, up_weight, down_weight):
    owners = lax.axis_size("expert")
    local_experts = up_weight.shape[0]
    experts = owners * local_experts
    tok_rows = tokens.shape[0]
    capacity = 2 * tok_rows // owners
    rows = experts * capacity
    slots = owners * capacity
    target = slot_targets(expert_ids, owners, local_experts, capacity)
    row_ids = lax.broadcasted_iota(jnp.int32, (rows, 2 * tok_rows), 0)
    placer = (row_ids == target[None, :]).astype(jnp.bfloat16)
    tok_ids = lax.broadcasted_iota(jnp.int32, (rows, tok_rows), 0)
    pair = target.reshape(tok_rows, 2)
    token_placer = ((tok_ids == pair[None, :, 0]) | (tok_ids == pair[None, :, 1])).astype(
        jnp.bfloat16
    )
    slot_gates = jnp.dot(
        placer.astype(jnp.float32),
        gates.reshape(-1),
        precision=lax.Precision.HIGHEST,
        preferred_element_type=jnp.float32,
    )

    whole_tokens = lax.all_gather(tokens, "ffn", axis=1, tiled=True)
    whole_cot = lax.all_gather(cotangent, "ffn", axis=1, tiled=True)

    def dispatch(send):
        send = send.reshape(local_experts, owners, capacity, *send.shape[1:])
        got = lax.all_to_all(send, "expert", split_axis=1, concat_axis=1, tiled=True)
        return got.reshape(local_experts, slots, *got.shape[3:])

    def place(whole):
        return jnp.dot(token_placer, whole, preferred_element_type=jnp.float32).astype(
            jnp.bfloat16
        )

    rows_in = dispatch(place(whole_tokens))
    scaled = slot_gates[:, None] * jnp.dot(
        token_placer, whole_cot, preferred_element_type=jnp.float32
    )
    rows_in, grads_send = lax.optimization_barrier((rows_in, scaled.astype(jnp.bfloat16)))
    grads_in = dispatch(grads_send)

    preact = jnp.einsum("xsd,xdf->xsf", rows_in, up_weight, preferred_element_type=jnp.float32)
    gating = jax.nn.sigmoid(preact)
    activated = (preact * gating).astype(jnp.bfloat16)
    out_part = [
        with_layout_constraint(
            jnp.einsum(
                "fd,sf->ds", down_weight[x], activated[x], preferred_element_type=jnp.float32
            ),
            Layout((0, 1)),
        ).astype(jnp.bfloat16)
        for x in range(local_experts)
    ]

    def send_home(parts):
        cols = jnp.stack(
            [lax.psum_scatter(part, "ffn", scatter_dimension=0, tiled=True) for part in parts],
            axis=1,
        )
        cols = cols.reshape(cols.shape[0], local_experts, owners, capacity)
        back = lax.all_to_all(cols, "expert", split_axis=2, concat_axis=2, tiled=True)
        return back.reshape(back.shape[0], rows)

    out_home = send_home(out_part)
    back_grad = jnp.einsum(
        "xsd,xfd->xsf", grads_in, down_weight, preferred_element_type=jnp.float32
    )
    pre_grad = (back_grad * gating * (1.0 + preact * (1.0 - gating))).astype(jnp.bfloat16)
    grad_down = jnp.einsum(
        "xsf,xsd->xfd", activated, grads_in, preferred_element_type=jnp.float32
    ).astype(jnp.bfloat16)
    grad_up = jnp.einsum(
        "xsd,xsf->xdf", rows_in, pre_grad, preferred_element_type=jnp.float32
    ).astype(jnp.bfloat16)
    in_part = [
        with_layout_constraint(
            jnp.einsum(
                "df,sf->ds", up_weight[x], pre_grad[x], preferred_element_type=jnp.float32
            ),
            Layout((0, 1)),
        ).astype(jnp.bfloat16)
        for x in range(local_experts)
    ]
    in_home = send_home(in_part)

    def gather_back(returned):
        picked = jnp.take(returned.T, target, axis=0).astype(jnp.float32)
        return picked.reshape(tok_rows, 2, returned.shape[0])

    layer_out = jnp.sum(gates[:, :, None] * gather_back(out_home), axis=1).astype(jnp.bfloat16)
    grad_tokens = jnp.sum(gather_back(in_home), axis=1).astype(jnp.bfloat16)
    return (layer_out, grad_tokens, grad_up, grad_down)


def solution(mesh):
    placed = (
        P("expert", "ffn"),
        P("expert", "ffn"),
        P("expert", None),
        P("expert", None),
        P("expert", None, "ffn"),
        P("expert", "ffn", None),
    )
    return jax.shard_map(
        shards,
        mesh=mesh,
        in_specs=placed,
        out_specs=(
            P("expert", "ffn"),
            P("expert", "ffn"),
            P("expert", None, "ffn"),
            P("expert", "ffn", None),
        ),
        check_vma=False,
    )
```
